32 devices in a mesh: groups: 2 (over x), rows: 16 (over z, y, core).
Axes of the slice: x: 2, y: 2, z: 4, core: 2. Of those that a mesh axis runs over, the one named last changes fastest.
Arguments:
- images: bfloat16 [32, 64, 3, 256], P('groups', 'rows'), parts along dimension 0, may hold values from -50 to 50
- shifts: int32 [32, 12], P('groups'), parts along dimension 0, may hold values from -48 to 48, as said below
- in_weight: bfloat16 [3, 3, 32, 3], replicated, may hold values from -1.25 to 1.25
- norm_gain: float32 [32], replicated, may hold values from 0.1 to 1.9
- norm_bias: float32 [32], replicated, may hold values from -3 to 3
- mid_weight: bfloat16 [3, 3, 32, 32], replicated, may hold values from -0.375 to 0.375
- out_weight: bfloat16 [3, 3, 32, 32], replicated, may hold values from -0.375 to 0.375
- cost_weight_a: bfloat16 [3, 3, 3, 32, 32], replicated, may hold values from -0.21875 to 0.21875
- cost_weight_b: bfloat16 [3, 3, 3, 32, 32], replicated, may hold values from -0.21875 to 0.21875
Outputs:
- regularized: bfloat16 [24, 64, 32, 256], P('groups', 'rows'), parts along dimension 0
The draws below stay inside these ranges and needn't reach their ends.
There are 2 independent parts, one for each index of `groups`. The reference program is written for one: setup_inputs(seed, part) draws one part's arguments, and reference() takes and returns one part's arrays. A program takes and returns all parts, laid end to end along the dimension named above; an argument that names none is the same for every part. Nothing has to cross between parts.
Inputs may be any that keep to these rules, and one draw needn't show every extreme that they name: `shifts`: the shift of camera v at plane k is b_v * (k + 1) for an integer baseline b_v of -4 to 4; some camera has b_v = 4 and another b_v = -4.
All inputs are finite; a program needn't handle non-finite values.
Results may differ from the reference program's by a relative error of at most 0.0076.
Values may be sent and summed in bfloat16 or wider, within the bound.
No kernel may reach another device: no remote copies, remote signals or barrier semaphores. Data moves between devices by JAX's collectives and lax.ppermute only.
A program may use at most 128 MiB of HBM per device.

```python
import math
import jax
import jax.numpy as jnp
from jax import lax

VIEWS = 16
C = 32
IN_CH = 3
PLANES = 12
COLS = 256
HEIGHT = 64


def draw_images(key, part):
    first_key, second_key = jax.random.split(key)
    position = jnp.arange(HEIGHT, dtype=jnp.float32) / max(HEIGHT - 1, 1)
    base = jnp.clip(jax.random.normal(first_key, (VIEWS, HEIGHT, IN_CH, COLS), jnp.float32), -4.0, 4.0)
    row_scale = jnp.exp(position * math.log(3.0))
    col_scale = jnp.exp(jax.random.uniform(second_key, (COLS,), jnp.float32, 0.0, math.log(10.0)))
    values = base * row_scale[None, :, None, None] * col_scale[None, None, None, :] / 4.0
    return values.astype(jnp.bfloat16)


def draw_shifts(key, part):
    first_key, second_key, third_key = jax.random.split(key, 3)
    baseline = jax.random.randint(first_key, (VIEWS,), -4, 5)
    first_view = jax.random.randint(second_key, (), 0, VIEWS)
    second_view = (first_view + 1 + jax.random.randint(third_key, (), 0, VIEWS - 1)) % VIEWS
    baseline = baseline.at[first_view].set(4).at[second_view].set(-4)
    steps_out = jnp.arange(PLANES, dtype=jnp.int32) + 1
    return (baseline[:, None] * steps_out[None, :]).astype(jnp.int32)


def noise(own_key, extent, deviation, limit, kind=jnp.bfloat16):
    entries = jax.random.normal(own_key, extent, jnp.float32) * deviation
    return jnp.minimum(jnp.maximum(entries, -limit), limit).astype(kind)


def setup_inputs(seed: int = 0, part: int = 0) -> dict:
    seeds = jax.random.split(jax.random.key(seed), 10)
    part_splits = jax.random.split(jax.random.fold_in(seeds[9], part), 10)
    images = draw_images(jax.random.fold_in(jax.random.fold_in(seeds[9], part), 71), part)
    shifts = draw_shifts(jax.random.fold_in(jax.random.fold_in(seeds[9], part), 71), part)
    in_weight = noise(seeds[2], (3, 3, C, IN_CH), (9 * IN_CH) ** -0.5, 1.25)
    norm_gain = jnp.clip(1.0 + 0.18 * jax.random.normal(seeds[3], (C,), jnp.float32), 0.1, 1.9)
    norm_bias = noise(seeds[4], (C,), 0.5, 3.0, jnp.float32)
    mid_weight = noise(seeds[5], (3, 3, C, C), (9 * C) ** -0.5, 0.375)
    out_weight = noise(seeds[6], (3, 3, C, C), (9 * C) ** -0.5, 0.375)
    cost_weight_a = noise(seeds[7], (3, 3, 3, C, C), (27 * C) ** -0.5, 0.21875)
    cost_weight_b = noise(seeds[8], (3, 3, 3, C, C), (27 * C) ** -0.5, 0.21875)
    return {"images": images, "shifts": shifts, "in_weight": in_weight, "norm_gain": norm_gain, "norm_bias": norm_bias, "mid_weight": mid_weight, "out_weight": out_weight, "cost_weight_a": cost_weight_a, "cost_weight_b": cost_weight_b}


def plane_conv(source, weight):
    height = source.shape[0]
    width = source.shape[2]
    padded = jnp.pad(source, ((1, 1), (0, 0), (1, 1)))
    summed = jnp.zeros((height, weight.shape[2], width), jnp.float32)
    for tap_row in range(3):
        for tap_col in range(3):
            summed = summed + jnp.einsum('oc,rcw->row', weight[tap_row, tap_col].astype(jnp.float32), padded[tap_row:tap_row + height, :, tap_col:tap_col + width], precision=lax.Precision.HIGHEST)
    return summed

def volume_conv(source, weight):
    depth = source.shape[0]
    height = source.shape[1]
    width = source.shape[3]
    padded = jnp.pad(source, ((1, 1), (1, 1), (0, 0), (1, 1)))
    summed = jnp.zeros((depth, height, weight.shape[3], width), jnp.float32)
    for tap_depth in range(3):
        for tap_row in range(3):
            for tap_col in range(3):
                summed = summed + jnp.einsum('oc,drcw->drow', weight[tap_depth, tap_row, tap_col].astype(jnp.float32), padded[tap_depth:tap_depth + depth, tap_row:tap_row + height, :, tap_col:tap_col + width], precision=lax.Precision.HIGHEST)
    return summed

def reference(images, shifts, in_weight, norm_gain, norm_bias, mid_weight, out_weight, cost_weight_a, cost_weight_b):

    def view_features(image):
        raw = plane_conv(image.astype(jnp.float32), in_weight)
        average = lax.optimization_barrier(jnp.mean(raw, axis=(0, 2)))
        centered = raw - average[None, :, None]
        spread = lax.optimization_barrier(jnp.mean(centered * centered, axis=(0, 2)))
        normed = jax.nn.relu(centered / jnp.sqrt(spread + 1e-05)[None, :, None] * norm_gain[None, :, None] + norm_bias[None, :, None]).astype(jnp.bfloat16)
        middle = jax.nn.relu(plane_conv(normed.astype(jnp.float32), mid_weight)).astype(jnp.bfloat16)
        return plane_conv(middle.astype(jnp.float32), out_weight).astype(jnp.bfloat16)
    features = lax.map(view_features, images)
    padding = 4 * PLANES
    padded = jnp.pad(features, ((0, 0), (0, 0), (0, 0), (padding, padding)))

    def one_plane(column):

        def take(view_feats, shift_by):
            return lax.dynamic_slice_in_dim(view_feats, (padding + shift_by).astype(jnp.int32), COLS, 2)
        warped = jax.vmap(take)(padded, column).astype(jnp.float32)
        average = lax.optimization_barrier(jnp.mean(warped, axis=0))
        return (lax.optimization_barrier(jnp.mean(warped * warped, axis=0)) - average * average).astype(jnp.bfloat16)
    volume = lax.map(one_plane, jnp.transpose(shifts))
    cost_hidden = jax.nn.relu(volume_conv(volume.astype(jnp.float32), cost_weight_a)).astype(jnp.bfloat16)
    return volume_conv(cost_hidden.astype(jnp.float32), cost_weight_b).astype(jnp.bfloat16)
```

```python
import jax
import jax.numpy as jnp
from jax import lax
from jax.sharding import PartitionSpec as P
from jax.experimental import pallas as pl
from jax.experimental.pallas import tpu as pltpu


def padded_2(cells, sides, width):
    for axis, dim in sides:
        count = lax.axis_size(axis)
        ends = count - 1
        head = lax.slice_in_dim(cells, 0, width, axis=dim)
        tail = lax.slice_in_dim(cells, cells.shape[dim] - width, cells.shape[dim], axis=dim)
        cells = jnp.concatenate(
            [
                lax.ppermute(tail, axis, [(i, (i + 1) % count) for i in range(ends)]),
                cells,
                lax.ppermute(head, axis, [((i + 1) % count, i) for i in range(ends)]),
            ],
            axis=dim,
        )
    return cells


def plane_conv(padded_rows, weight):
    rows_out = padded_rows.shape[1] - 2
    width = padded_rows.shape[3]
    padded = jnp.pad(padded_rows, ((0, 0), (0, 0), (0, 0), (1, 1)))
    summed = jnp.zeros((padded_rows.shape[0], rows_out, weight.shape[2], width), jnp.float32)
    for tap_row in range(3):
        for tap_col in range(3):
            summed = summed + jnp.einsum(
                "oc,vrcw->vrow",
                weight[tap_row, tap_col],
                padded[:, tap_row : tap_row + rows_out, :, tap_col : tap_col + width],
                preferred_element_type=jnp.float32,
            )
    return summed


def volume_conv(padded_rows, weight):
    depth = padded_rows.shape[0]
    rows_out = padded_rows.shape[1] - 2
    width = padded_rows.shape[3]
    padded = jnp.pad(padded_rows, ((1, 1), (0, 0), (0, 0), (1, 1)))
    summed = jnp.zeros((depth, rows_out, weight.shape[3], width), jnp.float32)
    for tap_depth in range(3):
        for tap_row in range(3):
            for tap_col in range(3):
                summed = summed + jnp.einsum(
                    "oc,drcw->drow",
                    weight[tap_depth, tap_row, tap_col],
                    padded[
                        tap_depth : tap_depth + depth,
                        tap_row : tap_row + rows_out,
                        :,
                        tap_col : tap_col + width,
                    ],
                    preferred_element_type=jnp.float32,
                )
    return summed


def variance_kernel(shift_ref, feats_ref, out_ref, total_ref, squares_ref):
    view = pl.program_id(0)
    view_count = pl.num_programs(0)
    plane_count = out_ref.shape[0]
    width = feats_ref.shape[2]

    @pl.when(view == 0)
    def _():
        total_ref[...] = jnp.zeros_like(total_ref)
        squares_ref[...] = jnp.zeros_like(squares_ref)

    feats = feats_ref[0].astype(jnp.float32)
    column = lax.broadcasted_iota(jnp.int32, feats.shape, 1)
    for plane in range(plane_count):
        shift = shift_ref[view, plane]
        rolled = pltpu.roll(feats, lax.rem(width - shift, width), 1)
        source = column + shift
        kept = jnp.where((source >= 0) & (source < width), rolled, 0.0)
        total_ref[plane] += kept
        squares_ref[plane] += kept * kept

    @pl.when(view == view_count - 1)
    def _():
        scale = 1.0 / view_count
        mean = total_ref[...] * scale
        out_ref[...] = (squares_ref[...] * scale - mean * mean).astype(out_ref.dtype)


def plane_variance(features, shifts):
    view_count, rows_here, channels, width = features.shape
    plane_count = shifts.shape[1]
    flat = features.reshape(view_count, rows_here * channels, width)
    grid_spec = pltpu.PrefetchScalarGridSpec(
        num_scalar_prefetch=1,
        grid=(view_count,),
        in_specs=[pl.BlockSpec((1, rows_here * channels, width), lambda v, s: (v, 0, 0))],
        out_specs=pl.BlockSpec((plane_count, rows_here * channels, width), lambda v, s: (0, 0, 0)),
        scratch_shapes=[
            pltpu.VMEM((plane_count, rows_here * channels, width), jnp.float32),
            pltpu.VMEM((plane_count, rows_here * channels, width), jnp.float32),
        ],
    )
    volume = pl.pallas_call(
        variance_kernel,
        grid_spec=grid_spec,
        out_shape=jax.ShapeDtypeStruct((plane_count, rows_here * channels, width), jnp.bfloat16),
        compiler_params=pltpu.CompilerParams(dimension_semantics=("arbitrary",)),
    )(shifts, flat)
    return volume.reshape(plane_count, rows_here, channels, width)


def shards(
    images,
    shifts,
    in_weight,
    norm_gain,
    norm_bias,
    mid_weight,
    out_weight,
    cost_weight_a,
    cost_weight_b,
):
    rows_here = images.shape[1]
    width = images.shape[3]
    count = rows_here * lax.axis_size("rows") * width
    rimmed = padded_2(images, (("rows", 1),), 1)
    raw = plane_conv(rimmed, in_weight)
    average = lax.psum(jnp.sum(raw, axis=(1, 3)), "rows") / count
    centered = raw - average[:, None, :, None]
    spread = lax.psum(jnp.sum(centered * centered, axis=(1, 3)), "rows") / count
    scaled = centered / jnp.sqrt(spread + 1e-05)[:, None, :, None]
    normed = jax.nn.relu(
        scaled * norm_gain[None, None, :, None] + norm_bias[None, None, :, None]
    ).astype(jnp.bfloat16)
    current = normed
    for layer, weight in enumerate((mid_weight, out_weight)):
        padded_rows = padded_2(current, (("rows", 1),), 1)
        result = plane_conv(padded_rows, weight)
        if layer == 0:
            result = jax.nn.relu(result)
        current = result.astype(jnp.bfloat16)
    features = current
    volume = plane_variance(features, shifts)
    current = volume
    for layer, weight in enumerate((cost_weight_a, cost_weight_b)):
        padded_rows = padded_2(current, (("rows", 1),), 1)
        result = volume_conv(padded_rows, weight)
        if layer == 0:
            result = jax.nn.relu(result)
        current = result.astype(jnp.bfloat16)
    return current


def solution(mesh):
    placed = (P("groups", "rows", None, None), P("groups", None), P(), P(), P(), P(), P(), P(), P())
    return jax.shard_map(
        shards,
        mesh=mesh,
        in_specs=placed,
        out_specs=P("groups", "rows", None, None),
        check_vma=False,
    )
```
